128 devices in a mesh: seq: 16 (over z, y), chan: 8 (over x, core).
Axes of the slice: x: 4, y: 4, z: 4, core: 2. Of those that a mesh axis runs over, the one named last changes fastest.
Arguments:
- query_projected: bfloat16 [4096, 4096], P('seq', 'chan'), may hold values from -6 to 6
- key_stream: bfloat16 [4096, 4096], P('seq', 'chan'), may hold values from -6 to 6
- value_stream: bfloat16 [4096, 4096], P('seq', 'chan'), may hold values from -6 to 6
- short_taps: float32 [3, 3, 4096], P(None, None, 'chan'), may hold values from -3 to 3
- skip_gain: float32 [4096], P('chan'), may hold values from -4 to 4
- long_filter: float32 [4096, 4096], P('seq', 'chan'), may hold values from -4 to 4
- out_weight: bfloat16 [4096, 4096], P('chan'), may hold values from -0.09375 to 0.09375
Outputs:
- mixed: bfloat16 [4096, 4096], P('seq')
The draws below stay inside these ranges and needn't reach their ends.
All inputs are finite; a program needn't handle non-finite values.
Results may differ from the reference program's by a relative error of at most 0.005.
Values may be sent and summed in bfloat16 or wider, within the bound.
No kernel may reach another device: no remote copies, remote signals or barrier semaphores. Data moves between devices by JAX's collectives and lax.ppermute only.
A program may use at most 128 MiB of HBM per device.

```python
import jax
import jax.numpy as jnp

EMBED_DIMENSION = 4096
SEQUENCE_EXTENT = 4096


def draw_long_filter(key, part):
    lookup_matrix = jax.random.split(key, 8)
    slow_share = 5
    slow = jax.random.randint(lookup_matrix[0], (EMBED_DIMENSION,), 0, 10) < slow_share
    fast_rate = 2.3 / jax.random.uniform(lookup_matrix[1], (EMBED_DIMENSION,), minval=30.0, maxval=50.0)
    slow_rate = 2.3 / SEQUENCE_EXTENT * jax.random.uniform(lookup_matrix[2], (EMBED_DIMENSION,), minval=0.05, maxval=0.4)
    rate = jnp.where(slow, slow_rate, fast_rate)
    lag_index = jnp.arange(SEQUENCE_EXTENT, dtype=jnp.int32)[:, None]
    lags = lag_index.astype(jnp.float32)
    envelope = jnp.exp(-rate[None, :] * lags)
    for impulse_amplitude in range(2):
        impulse_index = jax.random.randint(lookup_matrix[3 + impulse_amplitude], (EMBED_DIMENSION,), 1, SEQUENCE_EXTENT)
        falloff_factor = jax.random.uniform(lookup_matrix[5 + impulse_amplitude], (EMBED_DIMENSION,), minval=0.55, maxval=0.8)
        envelope = envelope * jnp.where(lag_index >= impulse_index[None, :], falloff_factor[None, :], 1.0)
    scale_norm = jnp.sqrt((1.0 - jnp.exp(-2.0 * rate * SEQUENCE_EXTENT)) / (1.0 - jnp.exp(-2.0 * rate)))
    noise = jnp.clip(jax.random.normal(lookup_matrix[7], (SEQUENCE_EXTENT, EMBED_DIMENSION), dtype=jnp.float32), -4.0, 4.0)
    return (noise * envelope / scale_norm[None, :]).astype(jnp.float32)


def shard_levels(key, shape, pieces, least, largest):
    level, own = 1.0, jax.random.fold_in(key, 6)
    for position, blocks in pieces:
        heights = jnp.exp(jax.random.uniform(jax.random.fold_in(own, position), (blocks,), jnp.float32, least / len(pieces), largest / len(pieces)))
        level = level * jnp.repeat(heights, shape[position] // blocks).reshape([-1 if axis == position else 1 for axis in range(len(shape))])
    return level


def bell_draw(key, extent, deviation, reach, cuts=(), kind=jnp.bfloat16):
    entries = jax.random.normal(key, extent, jnp.float32) * deviation
    if len(cuts) > 0:
        entries = shard_levels(key, extent, cuts, -0.22, 0.18) * entries
    return jnp.clip(entries, min=-reach, max=reach).astype(kind)


def setup_inputs(seed: int = 0) -> dict:
    streams_of = jax.random.split(jax.random.key(seed), 8)
    query_projected = bell_draw(streams_of[0], (SEQUENCE_EXTENT, EMBED_DIMENSION), 1.0, 6.0, ((0, 16), (1, 8)))
    key_stream = bell_draw(streams_of[1], (SEQUENCE_EXTENT, EMBED_DIMENSION), 1.0, 6.0, ((0, 16), (1, 8)))
    value_stream = bell_draw(streams_of[2], (SEQUENCE_EXTENT, EMBED_DIMENSION), 1.0, 6.0, ((0, 16), (1, 8)))
    short_taps = bell_draw(streams_of[3], (3, 3, EMBED_DIMENSION), 0.6, 3.0, ((2, 8),), jnp.float32)
    skip_gain = bell_draw(streams_of[4], (EMBED_DIMENSION,), 1.0, 4.0, ((0, 8),), jnp.float32)
    long_filter = draw_long_filter(jax.random.fold_in(streams_of[7], 71), 0)
    out_weight = bell_draw(streams_of[6], (EMBED_DIMENSION, EMBED_DIMENSION), EMBED_DIMENSION ** -0.5, 0.09375, ((0, 8),))
    return dict(query_projected=query_projected, key_stream=key_stream, value_stream=value_stream, short_taps=short_taps, skip_gain=skip_gain, long_filter=long_filter, out_weight=out_weight)


def causal_taps(field, weights):
    shift_one = jnp.concatenate([jnp.zeros_like(field[:1]), field[:-1]], axis=0)
    shift_two = jnp.concatenate([jnp.zeros_like(field[:2]), field[:-2]], axis=0)
    return weights[0] * field + weights[1] * shift_one + weights[2] * shift_two


def reference(query_projected, key_stream, value_stream, short_taps, skip_gain, long_filter, out_weight):
    shaped_q = causal_taps(query_projected.astype(jnp.float32), short_taps[:, 0])
    shaped_k = causal_taps(key_stream.astype(jnp.float32), short_taps[:, 1])
    shaped_v = causal_taps(value_stream.astype(jnp.float32), short_taps[:, 2])
    source = shaped_k * shaped_v
    padded_len = 2 * SEQUENCE_EXTENT
    product = jnp.fft.rfft(source, n=padded_len, axis=0) * jnp.fft.rfft(long_filter, n=padded_len, axis=0)
    convolved = jnp.fft.irfft(product, n=padded_len, axis=0)[:SEQUENCE_EXTENT].astype(jnp.float32)
    gated = (shaped_q * (convolved + skip_gain * source)).astype(jnp.bfloat16)
    return jnp.dot(gated, out_weight, preferred_element_type=jnp.float32).astype(jnp.bfloat16)
```

```python
import numpy as np

import jax
import jax.numpy as jnp
from jax import lax
from jax.sharding import PartitionSpec as P

HIGH = lax.Precision.HIGHEST


def dft_tables(seq_len):
    padded_len = 2 * seq_len
    rows = 64
    cols = padded_len // rows
    half_rows = rows // 2
    k1 = np.arange(rows)[:, None]
    n1 = np.arange(half_rows)[None, :]
    angle1 = 2.0 * np.pi * k1 * n1 / rows
    first = np.concatenate([np.cos(angle1), -np.sin(angle1)], axis=0)
    n2 = np.arange(cols)[None, :]
    angle_t = 2.0 * np.pi * k1 * n2 / padded_len
    twist = (np.cos(angle_t), np.sin(angle_t))
    k2 = np.arange(cols)[:, None]
    angle2 = 2.0 * np.pi * k2 * n2 / cols
    c2, s2 = np.cos(angle2), np.sin(angle2)
    forward = np.block([[c2, -s2], [s2, c2]])
    backward = np.block([[c2, s2], [-s2, c2]])
    last = np.concatenate([np.cos(angle1.T), -np.sin(angle1.T)], axis=1) / padded_len
    as32 = lambda a: jnp.asarray(a.astype(np.float32))
    return rows, cols, as32(first), tuple(as32(t) for t in twist), as32(forward), as32(backward), as32(last)


def spectrum(field, tables):
    rows, cols, first, twist, forward, _, _ = tables
    chans = field.shape[1]
    grid = field.reshape(rows // 2, cols, chans).transpose(0, 2, 1).reshape(rows // 2, chans * cols)
    stage = jnp.dot(first, grid, precision=HIGH).reshape(2, rows, chans, cols)
    tw_cos = twist[0][:, None, :]
    tw_sin = twist[1][:, None, :]
    turned_real = stage[0] * tw_cos + stage[1] * tw_sin
    turned_imag = stage[1] * tw_cos - stage[0] * tw_sin
    joined = jnp.concatenate([turned_real, turned_imag], axis=2).reshape(rows * chans, 2 * cols)
    return jnp.dot(joined, forward, precision=HIGH).reshape(rows, chans, 2 * cols)


def causal_conv(source, long_filter, tables):
    rows, cols, _, twist, _, backward, last = tables
    chans = source.shape[1]
    spec_s = spectrum(source, tables)
    spec_f = spectrum(long_filter, tables)
    sr, si = spec_s[..., :cols], spec_s[..., cols:]
    fr, fi = spec_f[..., :cols], spec_f[..., cols:]
    prod = jnp.concatenate([sr * fr - si * fi, sr * fi + si * fr], axis=2).reshape(rows * chans, 2 * cols)
    back = jnp.dot(prod, backward, precision=HIGH).reshape(rows, chans, 2 * cols)
    br, bi = back[..., :cols], back[..., cols:]
    tw_cos = twist[0][:, None, :]
    tw_sin = twist[1][:, None, :]
    turned_real = br * tw_cos - bi * tw_sin
    turned_imag = bi * tw_cos + br * tw_sin
    stacked = jnp.concatenate([turned_real, turned_imag], axis=0).reshape(2 * rows, chans * cols)
    out = jnp.dot(last, stacked, precision=HIGH).reshape(rows // 2, chans, cols)
    return out.transpose(0, 2, 1).reshape(rows // 2 * cols, chans)


def on_device(
    query_projected, key_stream, value_stream, short_taps, skip_gain, long_filter, out_weight
):
    seq_count = lax.axis_size("seq")
    place = lax.axis_index("seq")
    streams = jnp.stack([query_projected, key_stream, value_stream])
    full = lax.all_to_all(streams, "seq", 2, 1, tiled=True)
    filt = lax.all_to_all(long_filter, "seq", 1, 0, tiled=True)
    chans = full.shape[2]
    seq_len = full.shape[1]
    taps = lax.dynamic_slice_in_dim(short_taps, place * chans, chans, axis=2)
    gain = lax.dynamic_slice_in_dim(skip_gain, place * chans, chans, axis=0)
    x = full.astype(jnp.float32)
    zeros = jnp.zeros_like(x[:, :2])
    extended = jnp.concatenate([zeros, x], axis=1)
    shaped = (
        taps[0][:, None, :] * extended[:, 2:]
        + taps[1][:, None, :] * extended[:, 1:-1]
        + taps[2][:, None, :] * extended[:, :-2]
    )
    source = shaped[1] * shaped[2]
    tables = dft_tables(seq_len)
    convolved = causal_conv(source, filt, tables)
    gated = (shaped[0] * (convolved + gain[None, :] * source)).astype(jnp.bfloat16)
    gated = lax.all_to_all(gated, "seq", 0, 1, tiled=True)
    terms = jnp.dot(gated, out_weight, preferred_element_type=jnp.float32)
    summed = lax.psum_scatter(terms, "chan", scatter_dimension=1, tiled=True)
    return lax.all_gather(summed.astype(jnp.bfloat16), "chan", axis=1, tiled=True)


def solution(mesh):
    return jax.shard_map(
        on_device,
        mesh=mesh,
        in_specs=(
            P("seq", "chan"),
            P("seq", "chan"),
            P("seq", "chan"),
            P(None, None, "chan"),
            P("chan"),
            P("seq", "chan"),
            P("chan", None),
        ),
        out_specs=P("seq", None),
        check_vma=False,
    )
```

```python
import numpy as np

import jax
import jax.numpy as jnp
from jax import lax
from jax.sharding import PartitionSpec as P

HIGH = lax.Precision.HIGHEST


def dft_tables(seq_len):
    padded_len = 2 * seq_len
    rows = 64
    cols = padded_len // rows
    half_rows = rows // 2
    k1 = np.arange(rows)[:, None]
    n1 = np.arange(half_rows)[None, :]
    angle1 = 2.0 * np.pi * k1 * n1 / rows
    first = np.concatenate([np.cos(angle1), -np.sin(angle1)], axis=0)
    n2 = np.arange(cols)[None, :]
    angle_t = 2.0 * np.pi * k1 * n2 / padded_len
    twist = (np.cos(angle_t), np.sin(angle_t))
    k2 = np.arange(cols)[:, None]
    angle2 = 2.0 * np.pi * k2 * n2 / cols
    c2, s2 = np.cos(angle2), np.sin(angle2)
    forward = np.block([[c2, -s2], [s2, c2]])
    backward = np.block([[c2, s2], [-s2, c2]])
    last = np.concatenate([np.cos(angle1.T), -np.sin(angle1.T)], axis=1) / padded_len
    as32 = lambda a: jnp.asarray(a.astype(np.float32))
    return rows, cols, as32(first), tuple(as32(t) for t in twist), as32(forward), as32(backward), as32(last)


def spectrum(field, tables):
    rows, cols, first, twist, forward, _, _ = tables
    chans = field.shape[1]
    grid = field.reshape(rows // 2, cols, chans).transpose(0, 2, 1).reshape(rows // 2, chans * cols)
    stage = jnp.dot(first, grid, precision=HIGH).reshape(2, rows, chans, cols)
    tw_cos = twist[0][:, None, :]
    tw_sin = twist[1][:, None, :]
    turned_real = stage[0] * tw_cos + stage[1] * tw_sin
    turned_imag = stage[1] * tw_cos - stage[0] * tw_sin
    joined = jnp.concatenate([turned_real, turned_imag], axis=2).reshape(rows * chans, 2 * cols)
    return jnp.dot(joined, forward, precision=HIGH).reshape(rows, chans, 2 * cols)


def causal_conv(source, long_filter, tables):
    rows, cols, _, twist, _, backward, last = tables
    chans = source.shape[1]
    spec_s = spectrum(source, tables)
    spec_f = spectrum(long_filter, tables)
    sr, si = spec_s[..., :cols], spec_s[..., cols:]
    fr, fi = spec_f[..., :cols], spec_f[..., cols:]
    prod = jnp.concatenate([sr * fr - si * fi, sr * fi + si * fr], axis=2).reshape(rows * chans, 2 * cols)
    back = jnp.dot(prod, backward, precision=HIGH).reshape(rows, chans, 2 * cols)
    br, bi = back[..., :cols], back[..., cols:]
    tw_cos = twist[0][:, None, :]
    tw_sin = twist[1][:, None, :]
    turned_real = br * tw_cos - bi * tw_sin
    turned_imag = bi * tw_cos + br * tw_sin
    stacked = jnp.concatenate([turned_real, turned_imag], axis=0).reshape(2 * rows, chans * cols)
    out = jnp.dot(last, stacked, precision=HIGH).reshape(rows // 2, chans, cols)
    return out.transpose(0, 2, 1).reshape(rows // 2 * cols, chans)


def on_device(
    query_projected, key_stream, value_stream, short_taps, skip_gain, long_filter, out_weight
):
    seq_count = lax.axis_size("seq")
    place = lax.axis_index("seq")
    streams = jnp.stack([query_projected, key_stream, value_stream])
    full = lax.all_to_all(streams, "seq", 2, 1, tiled=True)
    filt = lax.all_to_all(long_filter, "seq", 1, 0, tiled=True)
    chans = full.shape[2]
    seq_len = full.shape[1]
    taps = lax.dynamic_slice_in_dim(short_taps, place * chans, chans, axis=2)
    gain = lax.dynamic_slice_in_dim(skip_gain, place * chans, chans, axis=0)
    x = full.astype(jnp.float32)
    zeros = jnp.zeros_like(x[:, :2])
    extended = jnp.concatenate([zeros, x], axis=1)
    shaped = (
        taps[0][:, None, :] * extended[:, 2:]
        + taps[1][:, None, :] * extended[:, 1:-1]
        + taps[2][:, None, :] * extended[:, :-2]
    )
    source = shaped[1] * shaped[2]
    tables = dft_tables(seq_len)
    convolved = causal_conv(source, filt, tables)
    gated = (shaped[0] * (convolved + gain[None, :] * source)).astype(jnp.bfloat16)
    gated = lax.all_to_all(gated, "seq", 0, 1, tiled=True)
    terms = jnp.dot(gated, out_weight, preferred_element_type=jnp.float32)
    summed = lax.psum_scatter(terms, "cc", scatter_dimension=1, tiled=True)
    summed = lax.psum_scatter(summed, "cx", scatter_dimension=1, tiled=True)
    rounded = lax.all_gather(summed.astype(jnp.bfloat16), "cx", axis=1, tiled=True)
    return lax.all_gather(rounded, "cc", axis=1, tiled=True)


def solution(mesh):
    seq_size, chan_size = mesh.devices.shape
    split = jax.sharding.Mesh(mesh.devices.reshape(seq_size, chan_size // 2, 2), ("seq", "cx", "cc"))
    chan = ("cx", "cc")
    return jax.shard_map(
        on_device,
        mesh=split,
        in_specs=(
            P("seq", chan),
            P("seq", chan),
            P("seq", chan),
            P(None, None, chan),
            P(chan),
            P("seq", chan),
            P(chan, None),
        ),
        out_specs=P("seq", None),
        check_vma=False,
    )
```

```python
import numpy as np

import jax
import jax.numpy as jnp
from jax import lax
from jax.sharding import PartitionSpec as P

HIGH = lax.Precision.HIGH


def dft_tables(seq_len):
    padded_len = 2 * seq_len
    rows = 64
    cols = padded_len // rows
    half_rows = rows // 2
    k1 = np.arange(rows)[:, None]
    n1 = np.arange(half_rows)[None, :]
    angle1 = 2.0 * np.pi * k1 * n1 / rows
    first = np.concatenate([np.cos(angle1), -np.sin(angle1)], axis=0)
    n2 = np.arange(cols)[None, :]
    angle_t = 2.0 * np.pi * k1 * n2 / padded_len
    twist = (np.cos(angle_t), np.sin(angle_t))
    k2 = np.arange(cols)[:, None]
    angle2 = 2.0 * np.pi * k2 * n2 / cols
    c2, s2 = np.cos(angle2), np.sin(angle2)
    forward = np.block([[c2, -s2], [s2, c2]])
    backward = np.block([[c2, s2], [-s2, c2]])
    last = np.concatenate([np.cos(angle1.T), -np.sin(angle1.T)], axis=1) / padded_len
    as32 = lambda a: jnp.asarray(a.astype(np.float32))
    return rows, cols, as32(first), tuple(as32(t) for t in twist), as32(forward), as32(backward), as32(last)


def spectrum(field, tables):
    rows, cols, first, twist, forward, _, _ = tables
    chans = field.shape[1]
    grid = field.reshape(rows // 2, cols, chans).transpose(0, 2, 1).reshape(rows // 2, chans * cols)
    stage = jnp.dot(first, grid, precision=HIGH).reshape(2, rows, chans, cols)
    tw_cos = twist[0][:, None, :]
    tw_sin = twist[1][:, None, :]
    turned_real = stage[0] * tw_cos + stage[1] * tw_sin
    turned_imag = stage[1] * tw_cos - stage[0] * tw_sin
    joined = jnp.concatenate([turned_real, turned_imag], axis=2).reshape(rows * chans, 2 * cols)
    return jnp.dot(joined, forward, precision=HIGH).reshape(rows, chans, 2 * cols)


def causal_conv(source, long_filter, tables):
    rows, cols, _, twist, _, backward, last = tables
    chans = source.shape[1]
    spec_s = spectrum(source, tables)
    spec_f = spectrum(long_filter, tables)
    sr, si = spec_s[..., :cols], spec_s[..., cols:]
    fr, fi = spec_f[..., :cols], spec_f[..., cols:]
    prod = jnp.concatenate([sr * fr - si * fi, sr * fi + si * fr], axis=2).reshape(rows * chans, 2 * cols)
    back = jnp.dot(prod, backward, precision=HIGH).reshape(rows, chans, 2 * cols)
    br, bi = back[..., :cols], back[..., cols:]
    tw_cos = twist[0][:, None, :]
    tw_sin = twist[1][:, None, :]
    turned_real = br * tw_cos - bi * tw_sin
    turned_imag = bi * tw_cos + br * tw_sin
    stacked = jnp.concatenate([turned_real, turned_imag], axis=0).reshape(2 * rows, chans * cols)
    out = jnp.dot(last, stacked, precision=HIGH).reshape(rows // 2, chans, cols)
    return out.transpose(0, 2, 1).reshape(rows // 2 * cols, chans)


def on_device(
    query_projected, key_stream, value_stream, short_taps, skip_gain, long_filter, out_weight
):
    seq_count = lax.axis_size("seq")
    place = lax.axis_index("seq")
    streams = jnp.stack([query_projected, key_stream, value_stream])
    full = lax.all_to_all(streams, "seq", 2, 1, tiled=True)
    filt = lax.all_to_all(long_filter, "seq", 1, 0, tiled=True)
    chans = full.shape[2]
    seq_len = full.shape[1]
    taps = lax.dynamic_slice_in_dim(short_taps, place * chans, chans, axis=2)
    gain = lax.dynamic_slice_in_dim(skip_gain, place * chans, chans, axis=0)
    x = full.astype(jnp.float32)
    zeros = jnp.zeros_like(x[:, :2])
    extended = jnp.concatenate([zeros, x], axis=1)
    shaped = (
        taps[0][:, None, :] * extended[:, 2:]
        + taps[1][:, None, :] * extended[:, 1:-1]
        + taps[2][:, None, :] * extended[:, :-2]
    )
    source = shaped[1] * shaped[2]
    tables = dft_tables(seq_len)
    convolved = causal_conv(source, filt, tables)
    gated = (shaped[0] * (convolved + gain[None, :] * source)).astype(jnp.bfloat16)
    gated = lax.all_to_all(gated, "seq", 0, 1, tiled=True)
    terms = jnp.dot(gated, out_weight, preferred_element_type=jnp.float32)
    return lax.psum(terms, "chan").astype(jnp.bfloat16)


def solution(mesh):
    return jax.shard_map(
        on_device,
        mesh=mesh,
        in_specs=(
            P("seq", "chan"),
            P("seq", "chan"),
            P("seq", "chan"),
            P(None, None, "chan"),
            P("chan"),
            P("seq", "chan"),
            P("chan", None),
        ),
        out_specs=P("seq", None),
        check_vma=False,
    )
```

```python
import numpy as np

import jax
import jax.numpy as jnp
from jax import lax
from jax.sharding import PartitionSpec as P

HIGH = lax.Precision.HIGH


def dft_tables(seq_len):
    padded_len = 2 * seq_len
    rows = 64
    cols = padded_len // rows
    half_rows = rows // 2
    k1 = np.arange(rows)[:, None]
    n1 = np.arange(half_rows)[None, :]
    angle1 = 2.0 * np.pi * k1 * n1 / rows
    first = np.concatenate([np.cos(angle1), -np.sin(angle1)], axis=0)
    n2 = np.arange(cols)[None, :]
    angle_t = 2.0 * np.pi * k1 * n2 / padded_len
    twist = (np.cos(angle_t), np.sin(angle_t))
    k2 = np.arange(cols)[:, None]
    angle2 = 2.0 * np.pi * k2 * n2 / cols
    c2, s2 = np.cos(angle2), np.sin(angle2)
    forward = np.block([[c2, -s2], [s2, c2]])
    backward = np.block([[c2, s2], [-s2, c2]])
    last = np.concatenate([np.cos(angle1.T), -np.sin(angle1.T)], axis=1) / padded_len
    as32 = lambda a: jnp.asarray(a.astype(np.float32))
    return rows, cols, as32(first), tuple(as32(t) for t in twist), as32(forward), as32(backward), as32(last)


def spectrum(field, tables):
    rows, cols, first, twist, forward, _, _ = tables
    chans = field.shape[1]
    grid = field.reshape(rows // 2, cols, chans).transpose(0, 2, 1).reshape(rows // 2, chans * cols)
    stage = jnp.dot(first, grid, precision=HIGH).reshape(2, rows, chans, cols)
    tw_cos = twist[0][:, None, :]
    tw_sin = twist[1][:, None, :]
    turned_real = stage[0] * tw_cos + stage[1] * tw_sin
    turned_imag = stage[1] * tw_cos - stage[0] * tw_sin
    joined = jnp.concatenate([turned_real, turned_imag], axis=2).reshape(rows * chans, 2 * cols)
    return jnp.dot(joined, forward, precision=HIGH).reshape(rows, chans, 2 * cols)


def causal_conv(source, long_filter, tables):
    rows, cols, _, twist, _, backward, last = tables
    chans = source.shape[1]
    spec_s = spectrum(source, tables)
    spec_f = spectrum(long_filter, tables)
    sr, si = spec_s[..., :cols], spec_s[..., cols:]
    fr, fi = spec_f[..., :cols], spec_f[..., cols:]
    prod = jnp.concatenate([sr * fr - si * fi, sr * fi + si * fr], axis=2).reshape(rows * chans, 2 * cols)
    back = jnp.dot(prod, backward, precision=HIGH).reshape(rows, chans, 2 * cols)
    br, bi = back[..., :cols], back[..., cols:]
    tw_cos = twist[0][:, None, :]
    tw_sin = twist[1][:, None, :]
    turned_real = br * tw_cos - bi * tw_sin
    turned_imag = bi * tw_cos + br * tw_sin
    stacked = jnp.concatenate([turned_real, turned_imag], axis=0).reshape(2 * rows, chans * cols)
    out = jnp.dot(last, stacked, precision=HIGH).reshape(rows // 2, chans, cols)
    return out.transpose(0, 2, 1).reshape(rows // 2 * cols, chans)


def on_device(
    query_projected, key_stream, value_stream, short_taps, skip_gain, long_filter, out_weight
):
    seq_count = lax.axis_size("seq")
    place = lax.axis_index("seq")
    shard_len, local_chans = query_projected.shape
    chans = local_chans // seq_count
    streams = jnp.stack([query_projected, key_stream, value_stream])
    streams = streams.reshape(3, shard_len, seq_count, chans).transpose(2, 0, 1, 3)
    full = lax.all_to_all(streams, "seq", 0, 0, tiled=True)
    full = full.transpose(1, 0, 2, 3).reshape(3, seq_count * shard_len, chans)
    filt = long_filter.reshape(shard_len, seq_count, chans).transpose(1, 0, 2)
    filt = lax.all_to_all(filt, "seq", 0, 0, tiled=True).reshape(seq_count * shard_len, chans)
    seq_len = full.shape[1]
    taps = lax.dynamic_slice_in_dim(short_taps, place * chans, chans, axis=2)
    gain = lax.dynamic_slice_in_dim(skip_gain, place * chans, chans, axis=0)
    x = full.astype(jnp.float32)
    zeros = jnp.zeros_like(x[:, :2])
    extended = jnp.concatenate([zeros, x], axis=1)
    shaped = (
        taps[0][:, None, :] * extended[:, 2:]
        + taps[1][:, None, :] * extended[:, 1:-1]
        + taps[2][:, None, :] * extended[:, :-2]
    )
    source = shaped[1] * shaped[2]
    tables = dft_tables(seq_len)
    convolved = causal_conv(source, filt, tables)
    gated = (shaped[0] * (convolved + gain[None, :] * source)).astype(jnp.bfloat16)
    gated = gated.reshape(seq_count, 2, shard_len // 2, chans)
    halves = []
    for half in range(2):
        back = lax.all_to_all(gated[:, half], "seq", 0, 0, tiled=True)
        back = back.transpose(1, 0, 2).reshape(shard_len // 2, local_chans)
        terms = jnp.dot(back, out_weight, preferred_element_type=jnp.float32)
        if halves:
            halves[-1], terms = lax.optimization_barrier((halves[-1], terms))
        halves.append(lax.psum(terms, "chan"))
    return jnp.concatenate(halves, axis=0).astype(jnp.bfloat16)


def solution(mesh):
    return jax.shard_map(
        on_device,
        mesh=mesh,
        in_specs=(
            P("seq", "chan"),
            P("seq", "chan"),
            P("seq", "chan"),
            P(None, None, "chan"),
            P("chan"),
            P("seq", "chan"),
            P("chan", None),
        ),
        out_specs=P("seq", None),
        check_vma=False,
    )
```

```python
import numpy as np

import jax
import jax.numpy as jnp
from jax import lax
from jax.sharding import PartitionSpec as P

HIGH = lax.Precision.HIGH


def dft_tables(seq_len):
    padded_len = 2 * seq_len
    rows = 64
    cols = padded_len // rows
    half_rows = rows // 2
    k1 = np.arange(rows)[:, None]
    n1 = np.arange(half_rows)[None, :]
    angle1 = 2.0 * np.pi * k1 * n1 / rows
    first = np.concatenate([np.cos(angle1), -np.sin(angle1)], axis=0)
    n2 = np.arange(cols)[None, :]
    angle_t = 2.0 * np.pi * k1 * n2 / padded_len
    twist = (np.cos(angle_t), np.sin(angle_t))
    k2 = np.arange(cols)[:, None]
    angle2 = 2.0 * np.pi * k2 * n2 / cols
    c2, s2 = np.cos(angle2), np.sin(angle2)
    forward = np.block([[c2, -s2], [s2, c2]])
    backward = np.block([[c2, s2], [-s2, c2]])
    last = np.concatenate([np.cos(angle1.T), -np.sin(angle1.T)], axis=1) / padded_len
    as32 = lambda a: jnp.asarray(a.astype(np.float32))
    return rows, cols, as32(first), tuple(as32(t) for t in twist), as32(forward), as32(backward), as32(last)


def spectrum(grid, tables):
    rows, cols, first, twist, forward, _, _ = tables
    chans = grid.shape[1]
    stage = jnp.dot(first, grid.reshape(rows // 2, chans * cols), precision=HIGH).reshape(2, rows, chans, cols)
    tw_cos = twist[0][:, None, :]
    tw_sin = twist[1][:, None, :]
    turned_real = stage[0] * tw_cos + stage[1] * tw_sin
    turned_imag = stage[1] * tw_cos - stage[0] * tw_sin
    joined = jnp.concatenate([turned_real, turned_imag], axis=2).reshape(rows * chans, 2 * cols)
    return jnp.dot(joined, forward, precision=HIGH).reshape(rows, chans, 2 * cols)


def causal_conv(source, long_filter, tables):
    rows, cols, _, twist, _, backward, last = tables
    chans = source.shape[1]
    spec_s = spectrum(source, tables)
    spec_f = spectrum(long_filter, tables)
    sr, si = spec_s[..., :cols], spec_s[..., cols:]
    fr, fi = spec_f[..., :cols], spec_f[..., cols:]
    prod = jnp.concatenate([sr * fr - si * fi, sr * fi + si * fr], axis=2).reshape(rows * chans, 2 * cols)
    back = jnp.dot(prod, backward, precision=HIGH).reshape(rows, chans, 2 * cols)
    br, bi = back[..., :cols], back[..., cols:]
    tw_cos = twist[0][:, None, :]
    tw_sin = twist[1][:, None, :]
    turned_real = br * tw_cos - bi * tw_sin
    turned_imag = bi * tw_cos + br * tw_sin
    stacked = jnp.concatenate([turned_real, turned_imag], axis=0).reshape(2 * rows, chans * cols)
    return jnp.dot(last, stacked, precision=HIGH).reshape(rows // 2, chans, cols)


def shift_back(grid, steps):
    prev = jnp.concatenate([jnp.zeros_like(grid[:, :1]), grid[:, :-1]], axis=1)
    cols = grid.shape[3]
    return jnp.concatenate([prev[..., cols - steps :], grid[..., : cols - steps]], axis=3)


def on_device(
    query_projected, key_stream, value_stream, short_taps, skip_gain, long_filter, out_weight
):
    seq_count = lax.axis_size("seq")
    place = lax.axis_index("seq")
    shard_len, local_chans = query_projected.shape
    chans = local_chans // seq_count
    tables = dft_tables(seq_count * shard_len)
    cols = tables[1]
    blocks = shard_len // cols
    streams = jnp.stack([query_projected, key_stream, value_stream])
    streams = streams.reshape(3, blocks, cols, seq_count, chans).transpose(3, 0, 1, 4, 2)
    full = lax.all_to_all(streams, "seq", 0, 0, tiled=True)
    full = full.transpose(1, 0, 2, 3, 4).reshape(3, seq_count * blocks, chans, cols)
    filt = long_filter.reshape(blocks, cols, seq_count, chans).transpose(2, 0, 3, 1)
    filt = lax.all_to_all(filt, "seq", 0, 0, tiled=True).reshape(seq_count * blocks, chans, cols)
    taps = lax.dynamic_slice_in_dim(short_taps, place * chans, chans, axis=2)
    gain = lax.dynamic_slice_in_dim(skip_gain, place * chans, chans, axis=0)
    x = full.astype(jnp.float32)
    shaped = (
        taps[0][:, None, :, None] * x
        + taps[1][:, None, :, None] * shift_back(x, 1)
        + taps[2][:, None, :, None] * shift_back(x, 2)
    )
    source = shaped[1] * shaped[2]
    convolved = causal_conv(source, filt, tables)
    gated = (shaped[0] * (convolved + gain[None, :, None] * source)).astype(jnp.bfloat16)
    gated = lax.all_to_all(gated.reshape(seq_count, blocks, chans, cols), "seq", 0, 0, tiled=True)
    gated = gated.transpose(1, 3, 0, 2).reshape(shard_len, local_chans)
    terms = jnp.dot(gated, out_weight, preferred_element_type=jnp.float32)
    return lax.psum(terms, "chan").astype(jnp.bfloat16)


def solution(mesh):
    return jax.shard_map(
        on_device,
        mesh=mesh,
        in_specs=(
            P("seq", "chan"),
            P("seq", "chan"),
            P("seq", "chan"),
            P(None, None, "chan"),
            P("chan"),
            P("seq", "chan"),
            P("chan", None),
        ),
        out_specs=P("seq", None),
        check_vma=False,
    )
```

```python
import numpy as np

import jax
import jax.numpy as jnp
from jax import lax
from jax.sharding import PartitionSpec as P

HIGH = lax.Precision.HIGH


def dft_tables(seq_len):
    padded_len = 2 * seq_len
    rows = 64
    cols = padded_len // rows
    half_rows = rows // 2
    k1 = np.arange(rows)[:, None]
    n1 = np.arange(half_rows)[None, :]
    angle1 = 2.0 * np.pi * k1 * n1 / rows
    first = np.concatenate([np.cos(angle1), -np.sin(angle1)], axis=0)
    n2 = np.arange(cols)[None, :]
    angle_t = 2.0 * np.pi * k1 * n2 / padded_len
    twist = (np.cos(angle_t), np.sin(angle_t))
    k2 = np.arange(cols)[:, None]
    angle2 = 2.0 * np.pi * k2 * n2 / cols
    c2, s2 = np.cos(angle2), np.sin(angle2)
    forward = np.block([[c2, -s2], [s2, c2]])
    backward = np.block([[c2, s2], [-s2, c2]])
    last = np.concatenate([np.cos(angle1.T), -np.sin(angle1.T)], axis=1) / padded_len
    as32 = lambda a: jnp.asarray(a.astype(np.float32))
    return rows, cols, as32(first), tuple(as32(t) for t in twist), as32(forward), as32(backward), as32(last)


def spectrum(grid, tables):
    rows, cols, first, twist, forward, _, _ = tables
    chans = grid.shape[1]
    stage = jnp.dot(first, grid.reshape(rows // 2, chans * cols), precision=HIGH).reshape(2, rows, chans, cols)
    tw_cos = twist[0][:, None, :]
    tw_sin = twist[1][:, None, :]
    turned_real = stage[0] * tw_cos + stage[1] * tw_sin
    turned_imag = stage[1] * tw_cos - stage[0] * tw_sin
    joined = jnp.concatenate([turned_real, turned_imag], axis=2).reshape(rows * chans, 2 * cols)
    return jnp.dot(joined, forward, precision=HIGH).reshape(rows, chans, 2 * cols)


def causal_conv(source, long_filter, tables):
    rows, cols, _, twist, _, backward, last = tables
    chans = source.shape[1]
    spec_s = spectrum(source, tables)
    spec_f = spectrum(long_filter, tables)
    sr, si = spec_s[..., :cols], spec_s[..., cols:]
    fr, fi = spec_f[..., :cols], spec_f[..., cols:]
    prod = jnp.concatenate([sr * fr - si * fi, sr * fi + si * fr], axis=2).reshape(rows * chans, 2 * cols)
    back = jnp.dot(prod, backward, precision=HIGH).reshape(rows, chans, 2 * cols)
    br, bi = back[..., :cols], back[..., cols:]
    tw_cos = twist[0][:, None, :]
    tw_sin = twist[1][:, None, :]
    turned_real = br * tw_cos - bi * tw_sin
    turned_imag = bi * tw_cos + br * tw_sin
    stacked = jnp.concatenate([turned_real, turned_imag], axis=0).reshape(2 * rows, chans * cols)
    return jnp.dot(last, stacked, precision=HIGH).reshape(rows // 2, chans, cols)


def shift_back(grid, steps):
    prev = jnp.concatenate([jnp.zeros_like(grid[:, :1]), grid[:, :-1]], axis=1)
    cols = grid.shape[3]
    return jnp.concatenate([prev[..., cols - steps :], grid[..., : cols - steps]], axis=3)


def on_device(
    query_projected, key_stream, value_stream, short_taps, skip_gain, long_filter, out_weight
):
    seq_count = lax.axis_size("seq")
    place = lax.axis_index("seq")
    shard_len, local_chans = query_projected.shape
    chans = local_chans // seq_count
    tables = dft_tables(seq_count * shard_len)
    cols = tables[1]
    blocks = shard_len // cols
    streams = jnp.stack([query_projected, key_stream, value_stream])
    streams = streams.reshape(3, blocks, cols, seq_count, chans).transpose(3, 0, 1, 4, 2)
    filt = long_filter.reshape(blocks, cols, seq_count, chans).transpose(2, 0, 3, 1)
    high = filt.astype(jnp.bfloat16)
    rest = filt - high.astype(jnp.float32)
    mid = rest.astype(jnp.bfloat16)
    low = (rest - mid.astype(jnp.float32)).astype(jnp.bfloat16)
    planes = jnp.concatenate([streams, jnp.stack([high, mid, low], axis=1)], axis=1)
    planes = lax.all_to_all(planes, "seq", 0, 0, tiled=True)
    full = planes[:, :3].transpose(1, 0, 2, 3, 4).reshape(3, seq_count * blocks, chans, cols)
    parts = planes[:, 3:].astype(jnp.float32)
    filt = ((parts[:, 0] + parts[:, 1]) + parts[:, 2]).reshape(seq_count * blocks, chans, cols)
    taps = lax.dynamic_slice_in_dim(short_taps, place * chans, chans, axis=2)
    gain = lax.dynamic_slice_in_dim(skip_gain, place * chans, chans, axis=0)
    x = full.astype(jnp.float32)
    shaped = (
        taps[0][:, None, :, None] * x
        + taps[1][:, None, :, None] * shift_back(x, 1)
        + taps[2][:, None, :, None] * shift_back(x, 2)
    )
    source = shaped[1] * shaped[2]
    convolved = causal_conv(source, filt, tables)
    gated = (shaped[0] * (convolved + gain[None, :, None] * source)).astype(jnp.bfloat16)
    gated = lax.all_to_all(gated.reshape(seq_count, blocks, chans, cols), "seq", 0, 0, tiled=True)
    gated = gated.transpose(1, 3, 0, 2).reshape(shard_len, local_chans)
    terms = jnp.dot(gated, out_weight, preferred_element_type=jnp.float32)
    return lax.psum(terms, "chan").astype(jnp.bfloat16)


def solution(mesh):
    return jax.shard_map(
        on_device,
        mesh=mesh,
        in_specs=(
            P("seq", "chan"),
            P("seq", "chan"),
            P("seq", "chan"),
            P(None, None, "chan"),
            P("chan"),
            P("seq", "chan"),
            P("chan", None),
        ),
        out_specs=P("seq", None),
        check_vma=False,
    )
```

```python
import numpy as np

import jax
import jax.numpy as jnp
from jax import lax
from jax.sharding import PartitionSpec as P

HIGH = lax.Precision.HIGH


def dft_tables(seq_len):
    padded_len = 2 * seq_len
    rows = 64
    cols = padded_len // rows
    half_rows = rows // 2
    k1 = np.arange(rows)[:, None]
    n1 = np.arange(half_rows)[None, :]
    angle1 = 2.0 * np.pi * k1 * n1 / rows
    first = np.concatenate([np.cos(angle1), -np.sin(angle1)], axis=0)
    n2 = np.arange(cols)[None, :]
    angle_t = 2.0 * np.pi * k1 * n2 / padded_len
    twist = (np.cos(angle_t), np.sin(angle_t))
    k2 = np.arange(cols)[:, None]
    angle2 = 2.0 * np.pi * k2 * n2 / cols
    c2, s2 = np.cos(angle2), np.sin(angle2)
    forward = np.block([[c2, -s2], [s2, c2]])
    backward = np.block([[c2, s2], [-s2, c2]])
    last = np.concatenate([np.cos(angle1.T), -np.sin(angle1.T)], axis=1) / padded_len
    as32 = lambda a: jnp.asarray(a.astype(np.float32))
    return rows, cols, as32(first), tuple(as32(t) for t in twist), as32(forward), as32(backward), as32(last)


def spectrum(grid, tables):
    rows, cols, first, twist, forward, _, _ = tables
    chans = grid.shape[1]
    stage = jnp.dot(first, grid.reshape(rows // 2, chans * cols), precision=HIGH).reshape(2, rows, chans, cols)
    tw_cos = twist[0][:, None, :]
    tw_sin = twist[1][:, None, :]
    turned_real = stage[0] * tw_cos + stage[1] * tw_sin
    turned_imag = stage[1] * tw_cos - stage[0] * tw_sin
    joined = jnp.concatenate([turned_real, turned_imag], axis=2).reshape(rows * chans, 2 * cols)
    return jnp.dot(joined, forward, precision=HIGH).reshape(rows, chans, 2 * cols)


def causal_conv(source, long_filter, tables):
    rows, cols, _, twist, _, backward, last = tables
    chans = source.shape[1]
    spec_s = spectrum(source, tables)
    spec_f = spectrum(long_filter, tables)
    sr, si = spec_s[..., :cols], spec_s[..., cols:]
    fr, fi = spec_f[..., :cols], spec_f[..., cols:]
    prod = jnp.concatenate([sr * fr - si * fi, sr * fi + si * fr], axis=2).reshape(rows * chans, 2 * cols)
    back = jnp.dot(prod, backward, precision=HIGH).reshape(rows, chans, 2 * cols)
    br, bi = back[..., :cols], back[..., cols:]
    tw_cos = twist[0][:, None, :]
    tw_sin = twist[1][:, None, :]
    turned_real = br * tw_cos - bi * tw_sin
    turned_imag = bi * tw_cos + br * tw_sin
    stacked = jnp.concatenate([turned_real, turned_imag], axis=0).reshape(2 * rows, chans * cols)
    return jnp.dot(last, stacked, precision=HIGH).reshape(rows // 2, chans, cols)


def shift_back(grid, steps):
    prev = jnp.concatenate([jnp.zeros_like(grid[:, :1]), grid[:, :-1]], axis=1)
    cols = grid.shape[3]
    return jnp.concatenate([prev[..., cols - steps :], grid[..., : cols - steps]], axis=3)


def on_device(
    query_projected, key_stream, value_stream, short_taps, skip_gain, long_filter, out_weight
):
    seq_count = lax.axis_size("seq")
    place = lax.axis_index("seq")
    shard_len, local_chans = query_projected.shape
    chans = local_chans // seq_count
    tables = dft_tables(seq_count * shard_len)
    cols = tables[1]
    blocks = shard_len // cols
    streams = jnp.stack([query_projected, key_stream, value_stream])
    streams = streams.reshape(3, blocks, cols, seq_count, chans).transpose(3, 0, 1, 4, 2)
    full = lax.all_to_all(streams, "seq", 0, 0, tiled=True)
    full = full.transpose(1, 0, 2, 3, 4).reshape(3, seq_count * blocks, chans, cols)
    filt = long_filter.reshape(blocks, cols, seq_count, chans).transpose(2, 0, 3, 1)
    filt = lax.all_to_all(filt, "seq", 0, 0, tiled=True).reshape(seq_count * blocks, chans, cols)
    taps = lax.dynamic_slice_in_dim(short_taps, place * chans, chans, axis=2)
    gain = lax.dynamic_slice_in_dim(skip_gain, place * chans, chans, axis=0)
    x = full.astype(jnp.float32)
    shaped = (
        taps[0][:, None, :, None] * x
        + taps[1][:, None, :, None] * shift_back(x, 1)
        + taps[2][:, None, :, None] * shift_back(x, 2)
    )
    source = shaped[1] * shaped[2]
    convolved = causal_conv(source, filt, tables)
    gated = (shaped[0] * (convolved + gain[None, :, None] * source)).astype(jnp.bfloat16)
    gated = gated.reshape(seq_count, blocks, chans, cols)
    halves = []
    for half in range(blocks):
        back = lax.all_to_all(gated[:, half], "seq", 0, 0, tiled=True)
        back = back.transpose(2, 0, 1).reshape(cols, local_chans)
        terms = jnp.dot(back, out_weight, preferred_element_type=jnp.float32)
        if halves:
            halves[-1], terms = lax.optimization_barrier((halves[-1], terms))
        halves.append(lax.psum(terms, "chan").astype(jnp.bfloat16))
    return jnp.concatenate(halves, axis=0)


def solution(mesh):
    return jax.shard_map(
        on_device,
        mesh=mesh,
        in_specs=(
            P("seq", "chan"),
            P("seq", "chan"),
            P("seq", "chan"),
            P(None, None, "chan"),
            P("chan"),
            P("seq", "chan"),
            P("chan", None),
        ),
        out_specs=P("seq", None),
        check_vma=False,
    )
```

```python
import numpy as np

import jax
import jax.numpy as jnp
from jax import lax
from jax.sharding import PartitionSpec as P

HIGH = lax.Precision.HIGH


def dft_tables(seq_len):
    padded_len = 2 * seq_len
    rows = 64
    cols = padded_len // rows
    half_rows = rows // 2
    k1 = np.arange(rows)[:, None]
    n1 = np.arange(half_rows)[None, :]
    angle1 = 2.0 * np.pi * k1 * n1 / rows
    first = np.concatenate([np.cos(angle1), -np.sin(angle1)], axis=0)
    n2 = np.arange(cols)[None, :]
    angle_t = 2.0 * np.pi * k1 * n2 / padded_len
    twist = (np.cos(angle_t), np.sin(angle_t))
    k2 = np.arange(cols)[:, None]
    angle2 = 2.0 * np.pi * k2 * n2 / cols
    c2, s2 = np.cos(angle2), np.sin(angle2)
    forward = np.block([[c2, -s2], [s2, c2]])
    backward = np.block([[c2, s2], [-s2, c2]])
    last = np.concatenate([np.cos(angle1.T), -np.sin(angle1.T)], axis=1) / padded_len
    as32 = lambda a: jnp.asarray(a.astype(np.float32))
    return rows, cols, as32(first), tuple(as32(t) for t in twist), as32(forward), as32(backward), as32(last)


def spectrum(grid, tables):
    rows, cols, first, twist, forward, _, _ = tables
    chans = grid.shape[1]
    stage = jnp.dot(first, grid.reshape(rows // 2, chans * cols), precision=HIGH).reshape(2, rows, chans, cols)
    tw_cos = twist[0][:, None, :]
    tw_sin = twist[1][:, None, :]
    turned_real = stage[0] * tw_cos + stage[1] * tw_sin
    turned_imag = stage[1] * tw_cos - stage[0] * tw_sin
    joined = jnp.concatenate([turned_real, turned_imag], axis=2).reshape(rows * chans, 2 * cols)
    return jnp.dot(joined, forward, precision=HIGH).reshape(rows, chans, 2 * cols)


def causal_conv(source, spec_f, tables):
    rows, cols, _, twist, _, backward, last = tables
    chans = source.shape[1]
    spec_s = spectrum(source, tables)
    sr, si = spec_s[..., :cols], spec_s[..., cols:]
    fr, fi = spec_f[..., :cols], spec_f[..., cols:]
    prod = jnp.concatenate([sr * fr - si * fi, sr * fi + si * fr], axis=2).reshape(rows * chans, 2 * cols)
    back = jnp.dot(prod, backward, precision=HIGH).reshape(rows, chans, 2 * cols)
    br, bi = back[..., :cols], back[..., cols:]
    tw_cos = twist[0][:, None, :]
    tw_sin = twist[1][:, None, :]
    turned_real = br * tw_cos - bi * tw_sin
    turned_imag = bi * tw_cos + br * tw_sin
    stacked = jnp.concatenate([turned_real, turned_imag], axis=0).reshape(2 * rows, chans * cols)
    return jnp.dot(last, stacked, precision=HIGH).reshape(rows // 2, chans, cols)


def shift_back(grid, steps):
    prev = jnp.concatenate([jnp.zeros_like(grid[:, :1]), grid[:, :-1]], axis=1)
    cols = grid.shape[3]
    return jnp.concatenate([prev[..., cols - steps :], grid[..., : cols - steps]], axis=3)


def on_device(
    query_projected, key_stream, value_stream, short_taps, skip_gain, long_filter, out_weight
):
    seq_count = lax.axis_size("seq")
    place = lax.axis_index("seq")
    shard_len, local_chans = query_projected.shape
    chans = local_chans // seq_count
    tables = dft_tables(seq_count * shard_len)
    cols = tables[1]
    blocks = shard_len // cols
    filt = long_filter.reshape(blocks, cols, seq_count, chans).transpose(2, 0, 3, 1)
    filt = lax.all_to_all(filt, "seq", 0, 0, tiled=True).reshape(seq_count * blocks, chans, cols)
    streams = jnp.stack([query_projected, key_stream, value_stream])
    streams = streams.reshape(3, blocks, cols, seq_count, chans).transpose(3, 0, 1, 4, 2)
    filt, streams = lax.optimization_barrier((filt, streams))
    spec_f = spectrum(filt, tables)
    full = lax.all_to_all(streams, "seq", 0, 0, tiled=True)
    spec_f, full = lax.optimization_barrier((spec_f, full))
    full = full.transpose(1, 0, 2, 3, 4).reshape(3, seq_count * blocks, chans, cols)
    taps = lax.dynamic_slice_in_dim(short_taps, place * chans, chans, axis=2)
    gain = lax.dynamic_slice_in_dim(skip_gain, place * chans, chans, axis=0)
    x = full.astype(jnp.float32)
    shaped = (
        taps[0][:, None, :, None] * x
        + taps[1][:, None, :, None] * shift_back(x, 1)
        + taps[2][:, None, :, None] * shift_back(x, 2)
    )
    source = shaped[1] * shaped[2]
    convolved = causal_conv(source, spec_f, tables)
    gated = (shaped[0] * (convolved + gain[None, :, None] * source)).astype(jnp.bfloat16)
    gated = lax.all_to_all(gated.reshape(seq_count, blocks, chans, cols), "seq", 0, 0, tiled=True)
    gated = gated.transpose(1, 3, 0, 2).reshape(shard_len, local_chans)
    terms = jnp.dot(gated, out_weight, preferred_element_type=jnp.float32)
    return lax.psum(terms, "chan").astype(jnp.bfloat16)


def solution(mesh):
    return jax.shard_map(
        on_device,
        mesh=mesh,
        in_specs=(
            P("seq", "chan"),
            P("seq", "chan"),
            P("seq", "chan"),
            P(None, None, "chan"),
            P("chan"),
            P("seq", "chan"),
            P("chan", None),
        ),
        out_specs=P("seq", None),
        check_vma=False,
    )
```

```python
import numpy as np

import jax
import jax.numpy as jnp
from jax import lax
from jax.sharding import PartitionSpec as P

HIGH = lax.Precision.HIGH


def dft_tables(seq_len):
    padded_len = 2 * seq_len
    rows = 64
    cols = padded_len // rows
    half_rows = rows // 2
    freqs = half_rows + 1
    k1 = np.arange(freqs)[:, None]
    n1 = np.arange(half_rows)[None, :]
    angle1 = 2.0 * np.pi * k1 * n1 / rows
    first = np.concatenate([np.cos(angle1), -np.sin(angle1)], axis=0)
    n2 = np.arange(cols)[None, :]
    angle_t = 2.0 * np.pi * k1 * n2 / padded_len
    twist = (np.cos(angle_t), np.sin(angle_t))
    k2 = np.arange(cols)[:, None]
    angle2 = 2.0 * np.pi * k2 * n2 / cols
    c2, s2 = np.cos(angle2), np.sin(angle2)
    forward = np.block([[c2, -s2], [s2, c2]])
    backward = np.block([[c2, s2], [-s2, c2]])
    weight = np.full(freqs, 2.0)
    weight[0] = weight[-1] = 1.0
    last = np.concatenate([np.cos(angle1.T) * weight, -np.sin(angle1.T) * weight], axis=1) / padded_len
    as32 = lambda a: jnp.asarray(a.astype(np.float32))
    return freqs, cols, as32(first), tuple(as32(t) for t in twist), as32(forward), as32(backward), as32(last)


def spectrum(grid, tables):
    rows, cols, first, twist, forward, _, _ = tables
    chans = grid.shape[1]
    stage = jnp.dot(first, grid.reshape(grid.shape[0], chans * cols), precision=HIGH).reshape(2, rows, chans, cols)
    tw_cos = twist[0][:, None, :]
    tw_sin = twist[1][:, None, :]
    turned_real = stage[0] * tw_cos + stage[1] * tw_sin
    turned_imag = stage[1] * tw_cos - stage[0] * tw_sin
    joined = jnp.concatenate([turned_real, turned_imag], axis=2).reshape(rows * chans, 2 * cols)
    return jnp.dot(joined, forward, precision=HIGH).reshape(rows, chans, 2 * cols)


def causal_conv(source, spec_f, tables):
    rows, cols, _, twist, _, backward, last = tables
    chans = source.shape[1]
    spec_s = spectrum(source, tables)
    sr, si = spec_s[..., :cols], spec_s[..., cols:]
    fr, fi = spec_f[..., :cols], spec_f[..., cols:]
    prod = jnp.concatenate([sr * fr - si * fi, sr * fi + si * fr], axis=2).reshape(rows * chans, 2 * cols)
    back = jnp.dot(prod, backward, precision=HIGH).reshape(rows, chans, 2 * cols)
    br, bi = back[..., :cols], back[..., cols:]
    tw_cos = twist[0][:, None, :]
    tw_sin = twist[1][:, None, :]
    turned_real = br * tw_cos - bi * tw_sin
    turned_imag = bi * tw_cos + br * tw_sin
    stacked = jnp.concatenate([turned_real, turned_imag], axis=0).reshape(2 * rows, chans * cols)
    return jnp.dot(last, stacked, precision=HIGH).reshape(last.shape[0], chans, cols)


def shift_back(grid, steps):
    prev = jnp.concatenate([jnp.zeros_like(grid[:, :1]), grid[:, :-1]], axis=1)
    cols = grid.shape[3]
    return jnp.concatenate([prev[..., cols - steps :], grid[..., : cols - steps]], axis=3)


def on_device(
    query_projected, key_stream, value_stream, short_taps, skip_gain, long_filter, out_weight
):
    seq_count = lax.axis_size("seq")
    place = lax.axis_index("seq")
    shard_len, local_chans = query_projected.shape
    chans = local_chans // seq_count
    tables = dft_tables(seq_count * shard_len)
    cols = tables[1]
    blocks = shard_len // cols
    filt = long_filter.reshape(blocks, cols, seq_count, chans).transpose(2, 0, 3, 1)
    filt = lax.all_to_all(filt, "seq", 0, 0, tiled=True).reshape(seq_count * blocks, chans, cols)
    streams = jnp.stack([query_projected, key_stream, value_stream])
    streams = streams.reshape(3, blocks, cols, seq_count, chans).transpose(3, 0, 1, 4, 2)
    filt, streams = lax.optimization_barrier((filt, streams))
    spec_f = spectrum(filt, tables)
    full = lax.all_to_all(streams, "seq", 0, 0, tiled=True)
    spec_f, full = lax.optimization_barrier((spec_f, full))
    full = full.transpose(1, 0, 2, 3, 4).reshape(3, seq_count * blocks, chans, cols)
    taps = lax.dynamic_slice_in_dim(short_taps, place * chans, chans, axis=2)
    gain = lax.dynamic_slice_in_dim(skip_gain, place * chans, chans, axis=0)
    x = full.astype(jnp.float32)
    shaped = (
        taps[0][:, None, :, None] * x
        + taps[1][:, None, :, None] * shift_back(x, 1)
        + taps[2][:, None, :, None] * shift_back(x, 2)
    )
    source = shaped[1] * shaped[2]
    convolved = causal_conv(source, spec_f, tables)
    gated = (shaped[0] * (convolved + gain[None, :, None] * source)).astype(jnp.bfloat16)
    gated = lax.all_to_all(gated.reshape(seq_count, blocks, chans, cols), "seq", 0, 0, tiled=True)
    gated = gated.transpose(1, 3, 0, 2).reshape(shard_len, local_chans)
    terms = jnp.dot(gated, out_weight, preferred_element_type=jnp.float32)
    return lax.psum(terms, "chan").astype(jnp.bfloat16)


def solution(mesh):
    return jax.shard_map(
        on_device,
        mesh=mesh,
        in_specs=(
            P("seq", "chan"),
            P("seq", "chan"),
            P("seq", "chan"),
            P(None, None, "chan"),
            P("chan"),
            P("seq", "chan"),
            P("chan", None),
        ),
        out_specs=P("seq", None),
        check_vma=False,
    )
```

```python
import numpy as np

import jax
import jax.numpy as jnp
from jax import lax
from jax.sharding import PartitionSpec as P

HIGH = lax.Precision.HIGHEST


def dft_tables(seq_len):
    padded_len = 2 * seq_len
    rows = 64
    cols = padded_len // rows
    half_rows = rows // 2
    freqs = half_rows + 1
    k1 = np.arange(freqs)[:, None]
    n1 = np.arange(half_rows)[None, :]
    angle1 = 2.0 * np.pi * k1 * n1 / rows
    first = np.concatenate([np.cos(angle1), -np.sin(angle1)], axis=0)
    n2 = np.arange(cols)[None, :]
    angle_t = 2.0 * np.pi * k1 * n2 / padded_len
    twist = (np.cos(angle_t), np.sin(angle_t))
    k2 = np.arange(cols)[:, None]
    angle2 = 2.0 * np.pi * k2 * n2 / cols
    c2, s2 = np.cos(angle2), np.sin(angle2)
    forward = np.block([[c2, -s2], [s2, c2]])
    backward = np.block([[c2, s2], [-s2, c2]])
    weight = np.full(freqs, 2.0)
    weight[0] = weight[-1] = 1.0
    last = np.concatenate([np.cos(angle1.T) * weight, -np.sin(angle1.T) * weight], axis=1) / padded_len
    as32 = lambda a: jnp.asarray(a.astype(np.float32))
    return freqs, cols, as32(first), tuple(as32(t) for t in twist), as32(forward), as32(backward), as32(last)


def spectrum(grid, tables):
    rows, cols, first, twist, forward, _, _ = tables
    chans = grid.shape[1]
    stage = jnp.dot(first, grid.reshape(grid.shape[0], chans * cols), precision=HIGH).reshape(2, rows, chans, cols)
    tw_cos = twist[0][:, None, :]
    tw_sin = twist[1][:, None, :]
    turned_real = stage[0] * tw_cos + stage[1] * tw_sin
    turned_imag = stage[1] * tw_cos - stage[0] * tw_sin
    joined = jnp.concatenate([turned_real, turned_imag], axis=2).reshape(rows * chans, 2 * cols)
    return jnp.dot(joined, forward, precision=HIGH).reshape(rows, chans, 2 * cols)


def causal_conv(source, spec_f, tables):
    rows, cols, _, twist, _, backward, last = tables
    chans = source.shape[1]
    spec_s = spectrum(source, tables)
    sr, si = spec_s[..., :cols], spec_s[..., cols:]
    fr, fi = spec_f[..., :cols], spec_f[..., cols:]
    prod = jnp.concatenate([sr * fr - si * fi, sr * fi + si * fr], axis=2).reshape(rows * chans, 2 * cols)
    back = jnp.dot(prod, backward, precision=HIGH).reshape(rows, chans, 2 * cols)
    br, bi = back[..., :cols], back[..., cols:]
    tw_cos = twist[0][:, None, :]
    tw_sin = twist[1][:, None, :]
    turned_real = br * tw_cos - bi * tw_sin
    turned_imag = bi * tw_cos + br * tw_sin
    stacked = jnp.concatenate([turned_real, turned_imag], axis=0).reshape(2 * rows, chans * cols)
    return jnp.dot(last, stacked, precision=HIGH).reshape(last.shape[0], chans, cols)


def shift_back(grid, steps):
    prev = jnp.concatenate([jnp.zeros_like(grid[:, :1]), grid[:, :-1]], axis=1)
    cols = grid.shape[3]
    return jnp.concatenate([prev[..., cols - steps :], grid[..., : cols - steps]], axis=3)


def on_device(
    query_projected, key_stream, value_stream, short_taps, skip_gain, long_filter, out_weight
):
    seq_count = lax.axis_size("seq")
    place = lax.axis_index("seq")
    shard_len, local_chans = query_projected.shape
    chans = local_chans // seq_count
    tables = dft_tables(seq_count * shard_len)
    cols = tables[1]
    blocks = shard_len // cols
    filt = long_filter.reshape(blocks, cols, seq_count, chans).transpose(2, 0, 3, 1)
    filt = lax.all_to_all(filt, "seq", 0, 0, tiled=True).reshape(seq_count * blocks, chans, cols)
    streams = jnp.stack([query_projected, key_stream, value_stream])
    streams = streams.reshape(3, blocks, cols, seq_count, chans).transpose(3, 0, 1, 4, 2)
    filt, streams = lax.optimization_barrier((filt, streams))
    spec_f = spectrum(filt, tables)
    full = lax.all_to_all(streams, "seq", 0, 0, tiled=True)
    spec_f, full = lax.optimization_barrier((spec_f, full))
    full = full.transpose(1, 0, 2, 3, 4).reshape(3, seq_count * blocks, chans, cols)
    taps = lax.dynamic_slice_in_dim(short_taps, place * chans, chans, axis=2)
    gain = lax.dynamic_slice_in_dim(skip_gain, place * chans, chans, axis=0)
    x = full.astype(jnp.float32)
    shaped = (
        taps[0][:, None, :, None] * x
        + taps[1][:, None, :, None] * shift_back(x, 1)
        + taps[2][:, None, :, None] * shift_back(x, 2)
    )
    source = shaped[1] * shaped[2]
    convolved = causal_conv(source, spec_f, tables)
    gated = (shaped[0] * (convolved + gain[None, :, None] * source)).astype(jnp.bfloat16)
    gated = lax.all_to_all(gated.reshape(seq_count, blocks, chans, cols), "seq", 0, 0, tiled=True)
    gated = gated.transpose(1, 3, 0, 2).reshape(shard_len, local_chans)
    terms = jnp.dot(gated, out_weight, preferred_element_type=jnp.float32)
    return lax.psum(terms, "chan").astype(jnp.bfloat16)


def solution(mesh):
    return jax.shard_map(
        on_device,
        mesh=mesh,
        in_specs=(
            P("seq", "chan"),
            P("seq", "chan"),
            P("seq", "chan"),
            P(None, None, "chan"),
            P("chan"),
            P("seq", "chan"),
            P("chan", None),
        ),
        out_specs=P("seq", None),
        check_vma=False,
    )
```

```python
import numpy as np

import jax
import jax.numpy as jnp
from jax import lax
from jax.sharding import PartitionSpec as P

HIGH = lax.Precision.HIGHEST


def dft_tables(seq_len):
    padded_len = 2 * seq_len
    rows = 64
    cols = padded_len // rows
    half_rows = rows // 2
    freqs = half_rows + 1
    k1 = np.arange(freqs)[:, None]
    n1 = np.arange(half_rows)[None, :]
    angle1 = 2.0 * np.pi * k1 * n1 / rows
    first = np.concatenate([np.cos(angle1), -np.sin(angle1)], axis=0)
    n2 = np.arange(cols)[None, :]
    angle_t = 2.0 * np.pi * k1 * n2 / padded_len
    twist = (np.cos(angle_t), np.sin(angle_t))
    k2 = np.arange(cols)[:, None]
    angle2 = 2.0 * np.pi * k2 * n2 / cols
    c2, s2 = np.cos(angle2), np.sin(angle2)
    forward = np.block([[c2, -s2], [s2, c2]])
    backward = np.block([[c2, s2], [-s2, c2]])
    weight = np.full(freqs, 2.0)
    weight[0] = weight[-1] = 1.0
    last = np.concatenate([np.cos(angle1.T) * weight, -np.sin(angle1.T) * weight], axis=1) / padded_len
    as32 = lambda a: jnp.asarray(a.astype(np.float32))
    return freqs, cols, as32(first), tuple(as32(t) for t in twist), as32(forward), as32(backward), as32(last)


def spectrum(grid, tables):
    rows, cols, first, twist, forward, _, _ = tables
    chans = grid.shape[1]
    stage = jnp.dot(first, grid.reshape(grid.shape[0], chans * cols), precision=HIGH).reshape(2, rows, chans, cols)
    tw_cos = twist[0][:, None, :]
    tw_sin = twist[1][:, None, :]
    turned_real = stage[0] * tw_cos + stage[1] * tw_sin
    turned_imag = stage[1] * tw_cos - stage[0] * tw_sin
    joined = jnp.concatenate([turned_real, turned_imag], axis=2).reshape(rows * chans, 2 * cols)
    return jnp.dot(joined, forward, precision=HIGH).reshape(rows, chans, 2 * cols)


def causal_conv(source, spec_f, tables):
    rows, cols, _, twist, _, backward, last = tables
    chans = source.shape[1]
    spec_s = spectrum(source, tables)
    sr, si = spec_s[..., :cols], spec_s[..., cols:]
    fr, fi = spec_f[..., :cols], spec_f[..., cols:]
    prod = jnp.concatenate([sr * fr - si * fi, sr * fi + si * fr], axis=2).reshape(rows * chans, 2 * cols)
    back = jnp.dot(prod, backward, precision=HIGH).reshape(rows, chans, 2 * cols)
    br, bi = back[..., :cols], back[..., cols:]
    tw_cos = twist[0][:, None, :]
    tw_sin = twist[1][:, None, :]
    turned_real = br * tw_cos - bi * tw_sin
    turned_imag = bi * tw_cos + br * tw_sin
    stacked = jnp.concatenate([turned_real, turned_imag], axis=0).reshape(2 * rows, chans * cols)
    return jnp.dot(last, stacked, precision=HIGH).reshape(last.shape[0], chans, cols)


def shift_back(grid, steps):
    prev = jnp.concatenate([jnp.zeros_like(grid[:, :1]), grid[:, :-1]], axis=1)
    cols = grid.shape[3]
    return jnp.concatenate([prev[..., cols - steps :], grid[..., : cols - steps]], axis=3)


def on_device(
    query_projected, key_stream, value_stream, short_taps, skip_gain, long_filter, out_weight
):
    seq_count = lax.axis_size("seq")
    place = lax.axis_index("seq")
    shard_len, local_chans = query_projected.shape
    chans = local_chans // seq_count
    tables = dft_tables(seq_count * shard_len)
    cols = tables[1]
    blocks = shard_len // cols
    filt = long_filter.reshape(blocks, cols, seq_count, chans).transpose(2, 0, 3, 1)
    filt = lax.all_to_all(filt.reshape(seq_count, blocks * chans, cols), "seq", 0, 0, tiled=True)
    filt = filt.reshape(seq_count * blocks, chans, cols)
    streams = jnp.stack([query_projected, key_stream, value_stream])
    streams = streams.reshape(3, blocks, cols, seq_count, chans).transpose(3, 0, 1, 4, 2)
    filt, streams = lax.optimization_barrier((filt, streams))
    spec_f = spectrum(filt, tables)
    full = lax.all_to_all(streams.reshape(seq_count, 3 * blocks * chans, cols), "seq", 0, 0, tiled=True)
    spec_f, full = lax.optimization_barrier((spec_f, full))
    full = full.reshape(seq_count, 3, blocks, chans, cols).transpose(1, 0, 2, 3, 4).reshape(3, seq_count * blocks, chans, cols)
    taps = lax.dynamic_slice_in_dim(short_taps, place * chans, chans, axis=2)
    gain = lax.dynamic_slice_in_dim(skip_gain, place * chans, chans, axis=0)
    x = full.astype(jnp.float32)
    shaped = (
        taps[0][:, None, :, None] * x
        + taps[1][:, None, :, None] * shift_back(x, 1)
        + taps[2][:, None, :, None] * shift_back(x, 2)
    )
    source = shaped[1] * shaped[2]
    convolved = causal_conv(source, spec_f, tables)
    gated = (shaped[0] * (convolved + gain[None, :, None] * source)).astype(jnp.bfloat16)
    gated = lax.all_to_all(gated.reshape(seq_count, blocks * chans, cols), "seq", 0, 0, tiled=True)
    gated = gated.reshape(seq_count, blocks, chans, cols).transpose(1, 3, 0, 2).reshape(shard_len, local_chans)
    terms = jnp.dot(gated, out_weight, preferred_element_type=jnp.float32)
    return lax.psum(terms, "chan").astype(jnp.bfloat16)


def solution(mesh):
    return jax.shard_map(
        on_device,
        mesh=mesh,
        in_specs=(
            P("seq", "chan"),
            P("seq", "chan"),
            P("seq", "chan"),
            P(None, None, "chan"),
            P("chan"),
            P("seq", "chan"),
            P("chan", None),
        ),
        out_specs=P("seq", None),
        check_vma=False,
    )
```

```python
import numpy as np

import jax
import jax.numpy as jnp
from jax import lax
from jax.sharding import PartitionSpec as P

HIGH = lax.Precision.HIGHEST


def dft_tables(seq_len):
    padded_len = 2 * seq_len
    rows = 64
    cols = padded_len // rows
    half_rows = rows // 2
    freqs = half_rows + 1
    k1 = np.arange(freqs)[:, None]
    n1 = np.arange(half_rows)[None, :]
    angle1 = 2.0 * np.pi * k1 * n1 / rows
    first = np.concatenate([np.cos(angle1), -np.sin(angle1)], axis=0)
    n2 = np.arange(cols)[None, :]
    angle_t = 2.0 * np.pi * k1 * n2 / padded_len
    twist = (np.cos(angle_t), np.sin(angle_t))
    k2 = np.arange(cols)[:, None]
    angle2 = 2.0 * np.pi * k2 * n2 / cols
    c2, s2 = np.cos(angle2), np.sin(angle2)
    forward = np.block([[c2, -s2], [s2, c2]])
    backward = np.block([[c2, s2], [-s2, c2]])
    weight = np.full(freqs, 2.0)
    weight[0] = weight[-1] = 1.0
    last = np.concatenate([np.cos(angle1.T) * weight, -np.sin(angle1.T) * weight], axis=1) / padded_len
    as32 = lambda a: jnp.asarray(a.astype(np.float32))
    return freqs, cols, as32(first), tuple(as32(t) for t in twist), as32(forward), as32(backward), as32(last)


def spectrum(grid, tables):
    rows, cols, first, twist, forward, _, _ = tables
    chans = grid.shape[1]
    stage = jnp.dot(first, grid.reshape(grid.shape[0], chans * cols), precision=HIGH).reshape(2, rows, chans, cols)
    tw_cos = twist[0][:, None, :]
    tw_sin = twist[1][:, None, :]
    turned_real = stage[0] * tw_cos + stage[1] * tw_sin
    turned_imag = stage[1] * tw_cos - stage[0] * tw_sin
    joined = jnp.concatenate([turned_real, turned_imag], axis=2).reshape(rows * chans, 2 * cols)
    return jnp.dot(joined, forward, precision=HIGH).reshape(rows, chans, 2 * cols)


def causal_conv(source, spec_f, tables):
    rows, cols, _, twist, _, backward, last = tables
    chans = source.shape[1]
    spec_s = spectrum(source, tables)
    sr, si = spec_s[..., :cols], spec_s[..., cols:]
    fr, fi = spec_f[..., :cols], spec_f[..., cols:]
    prod = jnp.concatenate([sr * fr - si * fi, sr * fi + si * fr], axis=2).reshape(rows * chans, 2 * cols)
    back = jnp.dot(prod, backward, precision=HIGH).reshape(rows, chans, 2 * cols)
    br, bi = back[..., :cols], back[..., cols:]
    tw_cos = twist[0][:, None, :]
    tw_sin = twist[1][:, None, :]
    turned_real = br * tw_cos - bi * tw_sin
    turned_imag = bi * tw_cos + br * tw_sin
    stacked = jnp.concatenate([turned_real, turned_imag], axis=0).reshape(2 * rows, chans * cols)
    return jnp.dot(last, stacked, precision=HIGH).reshape(last.shape[0], chans, cols)


def shift_back(grid, steps):
    prev = jnp.concatenate([jnp.zeros_like(grid[:, :1]), grid[:, :-1]], axis=1)
    cols = grid.shape[3]
    return jnp.concatenate([prev[..., cols - steps :], grid[..., : cols - steps]], axis=3)


def on_device(
    query_projected, key_stream, value_stream, short_taps, skip_gain, long_filter, out_weight
):
    seq_count = lax.axis_size("seq")
    place = lax.axis_index("seq")
    shard_len, local_chans = query_projected.shape
    chans = local_chans // seq_count
    tables = dft_tables(seq_count * shard_len)
    cols = tables[1]
    blocks = shard_len // cols
    filt = long_filter.reshape(blocks, cols, seq_count, chans).transpose(2, 0, 3, 1)
    filt = lax.all_to_all(filt, "seq", 0, 0, tiled=True).reshape(seq_count * blocks, chans, cols)
    streams = jnp.stack([query_projected, key_stream, value_stream])
    streams = streams.reshape(3, blocks, cols, seq_count, chans).transpose(3, 0, 1, 4, 2)
    spec_f = spectrum(filt, tables)
    full = lax.all_to_all(streams, "seq", 0, 0, tiled=True)
    spec_f, full = lax.optimization_barrier((spec_f, full))
    full = full.transpose(1, 0, 2, 3, 4).reshape(3, seq_count * blocks, chans, cols)
    taps = lax.dynamic_slice_in_dim(short_taps, place * chans, chans, axis=2)
    gain = lax.dynamic_slice_in_dim(skip_gain, place * chans, chans, axis=0)
    x = full.astype(jnp.float32)
    shaped = (
        taps[0][:, None, :, None] * x
        + taps[1][:, None, :, None] * shift_back(x, 1)
        + taps[2][:, None, :, None] * shift_back(x, 2)
    )
    source = shaped[1] * shaped[2]
    convolved = causal_conv(source, spec_f, tables)
    gated = (shaped[0] * (convolved + gain[None, :, None] * source)).astype(jnp.bfloat16)
    gated = lax.all_to_all(gated.reshape(seq_count, blocks, chans, cols), "seq", 0, 0, tiled=True)
    gated = gated.transpose(1, 3, 0, 2).reshape(shard_len, local_chans)
    terms = jnp.dot(gated, out_weight, preferred_element_type=jnp.float32)
    return lax.psum(terms, "chan").astype(jnp.bfloat16)


def solution(mesh):
    return jax.shard_map(
        on_device,
        mesh=mesh,
        in_specs=(
            P("seq", "chan"),
            P("seq", "chan"),
            P("seq", "chan"),
            P(None, None, "chan"),
            P("chan"),
            P("seq", "chan"),
            P("chan", None),
        ),
        out_specs=P("seq", None),
        check_vma=False,
    )
```

```python
import numpy as np

import jax
import jax.numpy as jnp
from jax import lax
from jax.sharding import PartitionSpec as P

HIGH = lax.Precision.HIGHEST


def dft_tables(seq_len):
    padded_len = 2 * seq_len
    rows = 64
    cols = padded_len // rows
    half_rows = rows // 2
    freqs = half_rows + 1
    k1 = np.arange(freqs)[:, None]
    n1 = np.arange(half_rows)[None, :]
    angle1 = 2.0 * np.pi * k1 * n1 / rows
    first = np.concatenate([np.cos(angle1), -np.sin(angle1)], axis=0)
    n2 = np.arange(cols)[None, :]
    angle_t = 2.0 * np.pi * k1 * n2 / padded_len
    twist = (np.cos(angle_t), np.sin(angle_t))
    k2 = np.arange(cols)[:, None]
    angle2 = 2.0 * np.pi * k2 * n2 / cols
    c2, s2 = np.cos(angle2), np.sin(angle2)
    forward = np.block([[c2, -s2], [s2, c2]])
    backward = np.block([[c2, s2], [-s2, c2]])
    weight = np.full(freqs, 2.0)
    weight[0] = weight[-1] = 1.0
    last = np.concatenate([np.cos(angle1.T) * weight, -np.sin(angle1.T) * weight], axis=1) / padded_len
    as32 = lambda a: jnp.asarray(a.astype(np.float32))
    return freqs, cols, as32(first), tuple(as32(t) for t in twist), as32(forward), as32(backward), as32(last)


def spectrum(grid, tables):
    rows, cols, first, twist, forward, _, _ = tables
    chans = grid.shape[1]
    stage = jnp.dot(first, grid.reshape(grid.shape[0], chans * cols), precision=HIGH).reshape(2, rows, chans, cols)
    tw_cos = twist[0][:, None, :]
    tw_sin = twist[1][:, None, :]
    turned_real = stage[0] * tw_cos + stage[1] * tw_sin
    turned_imag = stage[1] * tw_cos - stage[0] * tw_sin
    joined = jnp.concatenate([turned_real, turned_imag], axis=2).reshape(rows * chans, 2 * cols)
    return jnp.dot(joined, forward, precision=HIGH).reshape(rows, chans, 2 * cols)


def causal_conv(source, spec_f, tables):
    rows, cols, _, twist, _, backward, last = tables
    chans = source.shape[1]
    spec_s = spectrum(source, tables)
    sr, si = spec_s[..., :cols], spec_s[..., cols:]
    fr, fi = spec_f[..., :cols], spec_f[..., cols:]
    prod = jnp.concatenate([sr * fr - si * fi, sr * fi + si * fr], axis=2).reshape(rows * chans, 2 * cols)
    back = jnp.dot(prod, backward, precision=HIGH).reshape(rows, chans, 2 * cols)
    br, bi = back[..., :cols], back[..., cols:]
    tw_cos = twist[0][:, None, :]
    tw_sin = twist[1][:, None, :]
    turned_real = br * tw_cos - bi * tw_sin
    turned_imag = bi * tw_cos + br * tw_sin
    stacked = jnp.concatenate([turned_real, turned_imag], axis=0).reshape(2 * rows, chans * cols)
    return jnp.dot(last, stacked, precision=HIGH).reshape(last.shape[0], chans, cols)


def shift_back(grid, steps):
    prev = jnp.concatenate([jnp.zeros_like(grid[:, :1]), grid[:, :-1]], axis=1)
    cols = grid.shape[3]
    return jnp.concatenate([prev[..., cols - steps :], grid[..., : cols - steps]], axis=3)


def on_device(
    query_projected, key_stream, value_stream, short_taps, skip_gain, long_filter, out_weight
):
    seq_count = lax.axis_size("seq")
    place = lax.axis_index("seq")
    shard_len, local_chans = query_projected.shape
    chans = local_chans // seq_count
    tables = dft_tables(seq_count * shard_len)
    cols = tables[1]
    blocks = shard_len // cols
    filt = lax.all_to_all(long_filter, "seq", 1, 0, tiled=True)
    filt = filt.reshape(seq_count * blocks, cols, chans).transpose(0, 2, 1)
    streams = jnp.stack([query_projected, key_stream, value_stream])
    streams = streams.reshape(3, blocks, cols, seq_count, chans).transpose(3, 0, 1, 4, 2)
    spec_f = spectrum(filt, tables)
    full = lax.all_to_all(streams, "seq", 0, 0, tiled=True)
    spec_f, full = lax.optimization_barrier((spec_f, full))
    full = full.transpose(1, 0, 2, 3, 4).reshape(3, seq_count * blocks, chans, cols)
    taps = lax.dynamic_slice_in_dim(short_taps, place * chans, chans, axis=2)
    gain = lax.dynamic_slice_in_dim(skip_gain, place * chans, chans, axis=0)
    x = full.astype(jnp.float32)
    shaped = (
        taps[0][:, None, :, None] * x
        + taps[1][:, None, :, None] * shift_back(x, 1)
        + taps[2][:, None, :, None] * shift_back(x, 2)
    )
    source = shaped[1] * shaped[2]
    convolved = causal_conv(source, spec_f, tables)
    gated = (shaped[0] * (convolved + gain[None, :, None] * source)).astype(jnp.bfloat16)
    gated = lax.all_to_all(gated.reshape(seq_count, blocks, chans, cols), "seq", 0, 0, tiled=True)
    gated = gated.transpose(1, 3, 0, 2).reshape(shard_len, local_chans)
    terms = jnp.dot(gated, out_weight, preferred_element_type=jnp.float32)
    return lax.psum(terms, "chan").astype(jnp.bfloat16)


def solution(mesh):
    return jax.shard_map(
        on_device,
        mesh=mesh,
        in_specs=(
            P("seq", "chan"),
            P("seq", "chan"),
            P("seq", "chan"),
            P(None, None, "chan"),
            P("chan"),
            P("seq", "chan"),
            P("chan", None),
        ),
        out_specs=P("seq", None),
        check_vma=False,
    )
```
